768 devices in a mesh: atom: 96 (over y, z), energy: 8 (over x, core).
Axes of the slice: x: 4, y: 8, z: 12, core: 2. Of those that a mesh axis runs over, the one named last changes fastest.
Arguments:
- green: bfloat16 [192, 2, 12, 12, 1024], P('atom', None, None, None, 'energy'), may hold values from -6 to 6
- coupling: bfloat16 [192, 34, 2, 12, 12], P('atom'), may hold values from -0.5 to 0.5
- neighbours: int32 [192, 34], P('atom'), may hold values from 0 to 191, as said below
- offsets: int32 [70], replicated, may hold values from 1 to 48, as said below
- w_emit: float32 [70], replicated, may hold values from 0.02 to 0.2
- w_absorb: float32 [70], replicated, may hold values from 0.02 to 0.2
Outputs:
- self_energy: float32 [192, 2, 12, 12, 1024], P('atom', None, None, None, 'energy')
The draws below stay inside these ranges and needn't reach their ends.
Inputs may be any that keep to these rules, and one draw needn't show every extreme that they name: neighbours[a, k] lies among the atoms a // 2 - 1, a // 2, a // 2 + 1 times 2 plus 0 to 1, that is, among the atoms of the same index of atom or of an index one away. `offsets`: some frequency equals 48.
All inputs are finite; a program needn't handle non-finite values.
Results may differ from the reference program's by a relative error of at most 0.0028.
Values may be sent and summed in bfloat16 or wider, within the bound.
No kernel may reach another device: no remote copies, remote signals or barrier semaphores. Data moves between devices by JAX's collectives and lax.ppermute only.
A program may use at most 32 MiB of HBM per device.

```python
import math
import jax
import jax.numpy as jnp
from jax import lax

ORB = 12
NB = 34
NQ = 70
A_DEV = 2
OMAX = 48
ATOMS = 192
EN = 1024


def draw_neighbours(key, part):
    count = ATOMS // A_DEV
    keys = jax.random.split(jax.random.fold_in(key, 11), 4)
    owner = (jnp.arange(ATOMS, dtype=jnp.int32) // A_DEV)[:, None]
    limits = jax.random.randint(keys[0], (count,), 2, 7)
    limit_rows = jnp.repeat(limits, A_DEV)[:, None]
    chance = jax.random.randint(keys[1], (ATOMS, NB), 0, 8)
    side = jax.random.randint(keys[2], (ATOMS, NB), 0, 2) * 2 - 1
    moved = jnp.where(chance < limit_rows, side, 0)
    target = owner + moved
    moved = jnp.where((target < 0) | (target >= count), -moved, moved)
    within = jax.random.randint(keys[3], (ATOMS, NB), 0, A_DEV)
    return ((owner + moved) * A_DEV + within).astype(jnp.int32)


def draw_offsets(key, part):
    keys = jax.random.split(jax.random.fold_in(key, 23), 2)
    values = jax.random.randint(keys[0], (NQ,), 1, OMAX + 1)
    where_top = jax.random.randint(keys[1], (), 0, NQ)
    return values.at[where_top].set(OMAX).astype(jnp.int32)


def block_levels(key, extent, shards, least, top_value):
    level, own = 1.0, jax.random.fold_in(key, 6)
    for dim, shards_of in shards:
        steps = jnp.exp(jax.random.uniform(jax.random.fold_in(own, dim), (shards_of,), jnp.float32, least / len(shards), top_value / len(shards)))
        level = level * jnp.repeat(steps, extent[dim] // shards_of).reshape([-1 if axis == dim else 1 for axis in range(len(extent))])
    return level


def noise(own_key, dims, width, bound, cuts=(), kind=jnp.bfloat16):
    drawn = width * jax.random.normal(own_key, dims, jnp.float32)
    if cuts:
        drawn = drawn * block_levels(own_key, dims, cuts, -0.22, 0.18)
    return jnp.clip(drawn, -bound, bound).astype(kind)


def setup_inputs(seed: int = 0) -> dict:
    key_of = jax.random.split(jax.random.key(seed), 7)
    return {
        "green": noise(key_of[0], (ATOMS, 2, ORB, ORB, EN), 1.0, 6.0, ((0, 96), (4, 8))),
        "coupling": noise(key_of[1], (ATOMS, NB, 2, ORB, ORB), 140 ** -0.5, 0.5, ((0, 96),)),
        "neighbours": draw_neighbours(jax.random.fold_in(key_of[6], 71), 0),
        "offsets": draw_offsets(jax.random.fold_in(key_of[6], 71), 0),
        "w_emit": jnp.clip(jnp.exp(jax.random.uniform(key_of[4], (NQ,), jnp.float32, math.log(0.02), math.log(0.2))), 0.02, 0.2),
        "w_absorb": jnp.clip(jnp.exp(jax.random.uniform(key_of[5], (NQ,), jnp.float32, math.log(0.02), math.log(0.2))), 0.02, 0.2),
    }


def couple(blocks, gathered):
    hi = lax.Precision.HIGHEST
    coup = blocks.astype(jnp.float32)
    grn = gathered.astype(jnp.float32)
    x_re = jnp.einsum("kij,kjle->kile", coup[:, 0], grn[:, 0], precision=hi) - jnp.einsum("kij,kjle->kile", coup[:, 1], grn[:, 1], precision=hi)
    x_im = jnp.einsum("kij,kjle->kile", coup[:, 0], grn[:, 1], precision=hi) + jnp.einsum("kij,kjle->kile", coup[:, 1], grn[:, 0], precision=hi)
    x_re = lax.optimization_barrier(x_re.astype(jnp.bfloat16)).astype(jnp.float32)
    x_im = lax.optimization_barrier(x_im.astype(jnp.bfloat16)).astype(jnp.float32)
    p_re = jnp.einsum("kile,kml->ime", x_re, coup[:, 0], precision=hi) + jnp.einsum("kile,kml->ime", x_im, coup[:, 1], precision=hi)
    p_im = jnp.einsum("kile,kml->ime", x_im, coup[:, 0], precision=hi) - jnp.einsum("kile,kml->ime", x_re, coup[:, 1], precision=hi)
    return jnp.stack([p_re, p_im])


def reference(green, coupling, neighbours, offsets, w_emit, w_absorb):
    shifts = jnp.arange(-OMAX, OMAX + 1, dtype=jnp.int32)
    coeffs = jnp.sum(jnp.where(offsets[None, :] == shifts[:, None], w_emit[None, :], jnp.float32(0.0)), axis=1)
    coeffs = coeffs + jnp.sum(jnp.where(-offsets[None, :] == shifts[:, None], w_absorb[None, :], jnp.float32(0.0)), axis=1)

    def one_atom(packed):
        blocks, listed = packed
        gathered = jnp.take(green, listed, axis=0)
        coupled = couple(blocks, gathered).reshape(-1, EN)
        padded = jnp.pad(coupled, ((0, 0), (OMAX, OMAX)))

        def add_shift(index, total):
            return total + coeffs[index] * lax.dynamic_slice_in_dim(padded, index, EN, 1)

        total = lax.fori_loop(0, 2 * OMAX + 1, add_shift, jnp.zeros_like(coupled))
        return total.reshape(2, ORB, ORB, EN)

    return lax.map(one_atom, (coupling, neighbours))
```

```python
import jax
import jax.numpy as jnp
from jax import lax
from jax.sharding import PartitionSpec as P


def extended(cells, sides, width):
    for axis, dim in sides:
        count = lax.axis_size(axis)
        ends = count - 1
        head = lax.slice_in_dim(cells, 0, width, axis=dim)
        tail = lax.slice_in_dim(cells, cells.shape[dim] - width, cells.shape[dim], axis=dim)
        cells = jnp.concatenate(
            [
                lax.ppermute(tail, axis, [(i, (i + 1) % count) for i in range(ends)]),
                cells,
                lax.ppermute(head, axis, [((i + 1) % count, i) for i in range(ends)]),
            ],
            axis=dim,
        )
    return cells


def make_kernel(spread_diff, offsets, w_emit, w_absorb):
    kernel = jnp.sum(
        jnp.where(spread_diff[:, :, None] == offsets, w_emit, jnp.float32(0.0)), axis=2
    )
    return kernel + jnp.sum(
        jnp.where(spread_diff[:, :, None] == -offsets, w_absorb, jnp.float32(0.0)), axis=2
    )


def coupled_blocks(window, coupling, local_ids):
    f32, bf16 = jnp.float32, jnp.bfloat16
    nwin = window.shape[0]
    onehot = (local_ids[:, :, None] == jnp.arange(nwin, dtype=local_ids.dtype)).astype(bf16)
    mr = coupling[:, :, 0]
    mi = coupling[:, :, 1]
    mbig = jnp.stack([jnp.stack([mr, -mi], axis=2), jnp.stack([mi, mr], axis=2)], axis=2)
    left = mbig[:, :, :, None] * onehot[:, :, None, :, None, None, None]
    x = jnp.einsum("akqwpij,wpjle->akqile", left, window, preferred_element_type=f32).astype(bf16)
    x = x.transpose(0, 1, 2, 4, 3, 5)
    right = jnp.stack([jnp.stack([mr, mi], axis=2), jnp.stack([-mi, mr], axis=2)], axis=2)
    return jnp.einsum("akplie,akqpml->aqime", x, right, preferred_element_type=f32)


def shards(green, coupling, neighbours, offsets, w_emit, w_absorb):
    hi = lax.Precision.HIGHEST
    atoms_here = green.shape[0]
    points = green.shape[-1]
    reach = points * 3 // 8
    window = extended(green, (("atom", 0),), atoms_here)
    local_ids = neighbours - (lax.axis_index("atom") - 1) * atoms_here
    coupled = coupled_blocks(window, coupling, local_ids)

    extent = points + 2 * reach
    spread_diff = (
        jnp.arange(extent, dtype=jnp.int32)[:, None]
        - reach
        - jnp.arange(points, dtype=jnp.int32)[None, :]
    )
    kernel = make_kernel(spread_diff, offsets, w_emit, w_absorb)
    widened = extended(coupled, (("energy", 4),), reach)
    result = jnp.dot(
        widened.reshape(-1, extent), kernel, precision=hi, preferred_element_type=jnp.float32
    )
    return result.reshape(coupled.shape)


def solution(mesh):
    return jax.shard_map(
        shards,
        mesh=mesh,
        in_specs=(
            P("atom", None, None, None, "energy"),
            P("atom", None, None, None, None),
            P("atom", None),
            P(),
            P(),
            P(),
        ),
        out_specs=P("atom", None, None, None, "energy"),
        check_vma=False,
    )
```

```python
import jax
import jax.numpy as jnp
from jax import lax
from jax.sharding import PartitionSpec as P


def extended(cells, sides, width):
    for axis, dim in sides:
        count = lax.axis_size(axis)
        even = lax.axis_index(axis) % 2 == 0
        head = lax.slice_in_dim(cells, 0, width, axis=dim)
        tail = lax.slice_in_dim(cells, cells.shape[dim] - width, cells.shape[dim], axis=dim)
        edges = {
            parity: [(i, i + 1) for i in range(parity, count - 1, 2)]
            + [(i + 1, i) for i in range(parity, count - 1, 2)]
            for parity in (0, 1)
        }
        from_even = lax.ppermute(jnp.where(even, tail, head), axis, edges[0])
        from_odd = lax.ppermute(jnp.where(even, head, tail), axis, edges[1])
        cells = jnp.concatenate(
            [jnp.where(even, from_odd, from_even), cells, jnp.where(even, from_even, from_odd)],
            axis=dim,
        )
    return cells


def make_kernel(spread_diff, offsets, w_emit, w_absorb):
    kernel = jnp.sum(
        jnp.where(spread_diff[:, :, None] == offsets, w_emit, jnp.float32(0.0)), axis=2
    )
    return kernel + jnp.sum(
        jnp.where(spread_diff[:, :, None] == -offsets, w_absorb, jnp.float32(0.0)), axis=2
    )


def coupled_blocks(window, coupling, local_ids):
    f32, bf16 = jnp.float32, jnp.bfloat16
    nwin = window.shape[0]
    onehot = (local_ids[:, :, None] == jnp.arange(nwin, dtype=local_ids.dtype)).astype(bf16)
    mr = coupling[:, :, 0]
    mi = coupling[:, :, 1]
    mbig = jnp.stack([jnp.stack([mr, -mi], axis=2), jnp.stack([mi, mr], axis=2)], axis=2)
    left = mbig[:, :, :, None] * onehot[:, :, None, :, None, None, None]
    x = jnp.einsum("akqwpij,wpjle->akqile", left, window, preferred_element_type=f32).astype(bf16)
    x = x.transpose(0, 1, 2, 4, 3, 5)
    right = jnp.stack([jnp.stack([mr, mi], axis=2), jnp.stack([-mi, mr], axis=2)], axis=2)
    return jnp.einsum("akplie,akqpml->aqime", x, right, preferred_element_type=f32)


def shards(green, coupling, neighbours, offsets, w_emit, w_absorb):
    hi = lax.Precision.HIGHEST
    atoms_here = green.shape[0]
    points = green.shape[-1]
    reach = points * 3 // 8
    window = extended(green, (("atom", 0),), atoms_here)
    local_ids = neighbours - (lax.axis_index("atom") - 1) * atoms_here
    coupled = coupled_blocks(window, coupling, local_ids)

    extent = points + 2 * reach
    spread_diff = (
        jnp.arange(extent, dtype=jnp.int32)[:, None]
        - reach
        - jnp.arange(points, dtype=jnp.int32)[None, :]
    )
    kernel = make_kernel(spread_diff, offsets, w_emit, w_absorb)
    widened = extended(coupled, (("energy", 4),), reach)
    result = jnp.dot(
        widened.reshape(-1, extent), kernel, precision=hi, preferred_element_type=jnp.float32
    )
    return result.reshape(coupled.shape)


def solution(mesh):
    return jax.shard_map(
        shards,
        mesh=mesh,
        in_specs=(
            P("atom", None, None, None, "energy"),
            P("atom", None, None, None, None),
            P("atom", None),
            P(),
            P(),
            P(),
        ),
        out_specs=P("atom", None, None, None, "energy"),
        check_vma=False,
    )
```

```python
import jax
import jax.numpy as jnp
from jax import lax
from jax.sharding import PartitionSpec as P


def extended(cells, sides, width):
    for axis, dim in sides:
        count = lax.axis_size(axis)
        even = lax.axis_index(axis) % 2 == 0
        head = lax.slice_in_dim(cells, 0, width, axis=dim)
        tail = lax.slice_in_dim(cells, cells.shape[dim] - width, cells.shape[dim], axis=dim)
        edges = {
            parity: [(i, i + 1) for i in range(parity, count - 1, 2)]
            + [(i + 1, i) for i in range(parity, count - 1, 2)]
            for parity in (0, 1)
        }
        from_even = lax.ppermute(jnp.where(even, tail, head), axis, edges[0])
        from_odd = lax.ppermute(jnp.where(even, head, tail), axis, edges[1])
        cells = jnp.concatenate(
            [jnp.where(even, from_odd, from_even), cells, jnp.where(even, from_even, from_odd)],
            axis=dim,
        )
    return cells


def make_kernel(spread_diff, offsets, w_emit, w_absorb):
    kernel = jnp.sum(
        jnp.where(spread_diff[:, :, None] == offsets, w_emit, jnp.float32(0.0)), axis=2
    )
    return kernel + jnp.sum(
        jnp.where(spread_diff[:, :, None] == -offsets, w_absorb, jnp.float32(0.0)), axis=2
    )


def coupled_blocks(window, coupling, local_ids):
    f32, bf16 = jnp.float32, jnp.bfloat16
    nwin = window.shape[0]
    onehot = (local_ids[:, :, None] == jnp.arange(nwin, dtype=local_ids.dtype)).astype(bf16)
    mr = coupling[:, :, 0]
    mi = coupling[:, :, 1]
    mbig = jnp.stack([jnp.stack([mr, -mi], axis=2), jnp.stack([mi, mr], axis=2)], axis=2)
    left = mbig[:, :, :, None] * onehot[:, :, None, :, None, None, None]
    x = jnp.einsum("akqwpij,wpjle->akqile", left, window, preferred_element_type=f32).astype(bf16)
    x = x.transpose(0, 1, 2, 4, 3, 5)
    right = jnp.stack([jnp.stack([mr, mi], axis=2), jnp.stack([-mi, mr], axis=2)], axis=2)
    return jnp.einsum("akplie,akqpml->aqime", x, right, preferred_element_type=f32)


def shards(green, coupling, neighbours, offsets, w_emit, w_absorb):
    hi = lax.Precision.HIGHEST
    atoms_here = green.shape[0]
    points = green.shape[-1]
    reach = points * 3 // 8
    window = extended(green, (("energy", 4),), reach)
    window = extended(window, (("atom", 0),), atoms_here)
    local_ids = neighbours - (lax.axis_index("atom") - 1) * atoms_here
    widened = coupled_blocks(window, coupling, local_ids)

    extent = points + 2 * reach
    spread_diff = (
        jnp.arange(extent, dtype=jnp.int32)[:, None]
        - reach
        - jnp.arange(points, dtype=jnp.int32)[None, :]
    )
    kernel = make_kernel(spread_diff, offsets, w_emit, w_absorb)
    result = jnp.dot(
        widened.reshape(-1, extent), kernel, precision=hi, preferred_element_type=jnp.float32
    )
    return result.reshape(widened.shape[:-1] + (points,))


def solution(mesh):
    return jax.shard_map(
        shards,
        mesh=mesh,
        in_specs=(
            P("atom", None, None, None, "energy"),
            P("atom", None, None, None, None),
            P("atom", None),
            P(),
            P(),
            P(),
        ),
        out_specs=P("atom", None, None, None, "energy"),
        check_vma=False,
    )
```

```python
import jax
import jax.numpy as jnp
from jax import lax
from jax.sharding import PartitionSpec as P


def extended(cells, sides, width):
    for axis, dim in sides:
        count = lax.axis_size(axis)
        even = lax.axis_index(axis) % 2 == 0
        head = lax.slice_in_dim(cells, 0, width, axis=dim)
        tail = lax.slice_in_dim(cells, cells.shape[dim] - width, cells.shape[dim], axis=dim)
        edges = {
            parity: [(i, i + 1) for i in range(parity, count - 1, 2)]
            + [(i + 1, i) for i in range(parity, count - 1, 2)]
            for parity in (0, 1)
        }
        from_even = lax.ppermute(jnp.where(even, tail, head), axis, edges[0])
        from_odd = lax.ppermute(jnp.where(even, head, tail), axis, edges[1])
        cells = jnp.concatenate(
            [jnp.where(even, from_odd, from_even), cells, jnp.where(even, from_even, from_odd)],
            axis=dim,
        )
    return cells


def make_kernel(spread_diff, offsets, w_emit, w_absorb):
    kernel = jnp.sum(
        jnp.where(spread_diff[:, :, None] == offsets, w_emit, jnp.float32(0.0)), axis=2
    )
    return kernel + jnp.sum(
        jnp.where(spread_diff[:, :, None] == -offsets, w_absorb, jnp.float32(0.0)), axis=2
    )


def coupled_blocks(window, coupling, local_ids):
    f32, bf16 = jnp.float32, jnp.bfloat16
    nwin = window.shape[0]
    onehot = (local_ids[:, :, None] == jnp.arange(nwin, dtype=local_ids.dtype)).astype(bf16)
    mr = coupling[:, :, 0]
    mi = coupling[:, :, 1]
    mbig = jnp.stack([jnp.stack([mr, -mi], axis=2), jnp.stack([mi, mr], axis=2)], axis=2)
    left = mbig[:, :, :, None] * onehot[:, :, None, :, None, None, None]
    x = jnp.einsum("akqwpij,wpjle->akqile", left, window, preferred_element_type=f32).astype(bf16)
    x = x.transpose(0, 1, 2, 4, 3, 5)
    right = jnp.stack([jnp.stack([mr, mi], axis=2), jnp.stack([-mi, mr], axis=2)], axis=2)
    return jnp.einsum("akplie,akqpml->aqime", x, right, preferred_element_type=f32)


def shards(green, coupling, neighbours, offsets, w_emit, w_absorb):
    hi = lax.Precision.HIGHEST
    atoms_here = green.shape[0]
    points = green.shape[-1]
    reach = points * 3 // 8
    window = extended(green, (("atom", 0),), atoms_here)
    local_ids = neighbours - (lax.axis_index("atom") - 1) * atoms_here
    extent = points + 2 * reach
    spread_diff = (
        jnp.arange(extent, dtype=jnp.int32)[:, None]
        - reach
        - jnp.arange(points, dtype=jnp.int32)[None, :]
    )
    kernel = make_kernel(spread_diff, offsets, w_emit, w_absorb)
    coupled = coupled_blocks(window, coupling, local_ids)
    coupled, kernel = lax.optimization_barrier((coupled, kernel))
    widened = extended(coupled, (("energy", 4),), reach)
    result = jnp.dot(
        widened.reshape(-1, extent), kernel, precision=hi, preferred_element_type=jnp.float32
    )
    return result.reshape(coupled.shape)


def solution(mesh):
    return jax.shard_map(
        shards,
        mesh=mesh,
        in_specs=(
            P("atom", None, None, None, "energy"),
            P("atom", None, None, None, None),
            P("atom", None),
            P(),
            P(),
            P(),
        ),
        out_specs=P("atom", None, None, None, "energy"),
        check_vma=False,
    )
```

```python
import jax
import jax.numpy as jnp
from jax import lax
from jax.sharding import PartitionSpec as P


def extended(cells, sides, width):
    for axis, dim in sides:
        count = lax.axis_size(axis)
        even = lax.axis_index(axis) % 2 == 0
        head = lax.slice_in_dim(cells, 0, width, axis=dim)
        tail = lax.slice_in_dim(cells, cells.shape[dim] - width, cells.shape[dim], axis=dim)
        edges = {
            parity: [(i, i + 1) for i in range(parity, count - 1, 2)]
            + [(i + 1, i) for i in range(parity, count - 1, 2)]
            for parity in (0, 1)
        }
        from_even = lax.ppermute(jnp.where(even, tail, head), axis, edges[0])
        from_odd = lax.ppermute(jnp.where(even, head, tail), axis, edges[1])
        cells = jnp.concatenate(
            [jnp.where(even, from_odd, from_even), cells, jnp.where(even, from_even, from_odd)],
            axis=dim,
        )
    return cells


def make_kernel(spread_diff, offsets, w_emit, w_absorb):
    kernel = jnp.sum(
        jnp.where(spread_diff[:, :, None] == offsets, w_emit, jnp.float32(0.0)), axis=2
    )
    return kernel + jnp.sum(
        jnp.where(spread_diff[:, :, None] == -offsets, w_absorb, jnp.float32(0.0)), axis=2
    )


def coupled_blocks(window, coupling, local_ids):
    f32, bf16 = jnp.float32, jnp.bfloat16
    nwin = window.shape[0]
    onehot = (local_ids[:, :, None] == jnp.arange(nwin, dtype=local_ids.dtype)).astype(bf16)
    mr = coupling[:, :, 0]
    mi = coupling[:, :, 1]
    mbig = jnp.stack([jnp.stack([mr, -mi], axis=2), jnp.stack([mi, mr], axis=2)], axis=2)
    left = mbig[:, :, :, None] * onehot[:, :, None, :, None, None, None]
    x = jnp.einsum("akqwpij,wpjle->akqile", left, window, preferred_element_type=f32).astype(bf16)
    x = x.transpose(0, 1, 2, 4, 3, 5)
    right = jnp.stack([jnp.stack([mr, mi], axis=2), jnp.stack([-mi, mr], axis=2)], axis=2)
    return jnp.einsum("akplie,akqpml->aqime", x, right, preferred_element_type=f32)


def shards(green, coupling, neighbours, offsets, w_emit, w_absorb):
    hi = lax.Precision.HIGHEST
    atoms_here = green.shape[0]
    points = green.shape[-1]
    reach = points * 3 // 8
    window = extended(green, (("atom", 0),), atoms_here)
    local_ids = neighbours - (lax.axis_index("atom") - 1) * atoms_here
    extent = points + 2 * reach
    spread_diff = (
        jnp.arange(extent, dtype=jnp.int32)[:, None]
        - reach
        - jnp.arange(points, dtype=jnp.int32)[None, :]
    )
    kernel = make_kernel(spread_diff, offsets, w_emit, w_absorb)
    coupled = coupled_blocks(window, coupling, local_ids)
    coupled, kernel = lax.optimization_barrier((coupled, kernel))
    halo = extended(coupled.astype(jnp.bfloat16), (("energy", 4),), reach)
    widened = jnp.concatenate(
        [
            lax.slice_in_dim(halo, 0, reach, axis=4).astype(jnp.float32),
            coupled,
            lax.slice_in_dim(halo, halo.shape[4] - reach, halo.shape[4], axis=4).astype(jnp.float32),
        ],
        axis=4,
    )
    result = jnp.dot(
        widened.reshape(-1, extent), kernel, precision=hi, preferred_element_type=jnp.float32
    )
    return result.reshape(coupled.shape)


def solution(mesh):
    return jax.shard_map(
        shards,
        mesh=mesh,
        in_specs=(
            P("atom", None, None, None, "energy"),
            P("atom", None, None, None, None),
            P("atom", None),
            P(),
            P(),
            P(),
        ),
        out_specs=P("atom", None, None, None, "energy"),
        check_vma=False,
    )
```

```python
import jax
import jax.numpy as jnp
from jax import lax
from jax.sharding import PartitionSpec as P


def extended(cells, sides, width):
    for axis, dim in sides:
        count = lax.axis_size(axis)
        even = lax.axis_index(axis) % 2 == 0
        head = lax.slice_in_dim(cells, 0, width, axis=dim)
        tail = lax.slice_in_dim(cells, cells.shape[dim] - width, cells.shape[dim], axis=dim)
        edges = {
            parity: [(i, i + 1) for i in range(parity, count - 1, 2)]
            + [(i + 1, i) for i in range(parity, count - 1, 2)]
            for parity in (0, 1)
        }
        from_even = lax.ppermute(jnp.where(even, tail, head), axis, edges[0])
        from_odd = lax.ppermute(jnp.where(even, head, tail), axis, edges[1])
        cells = jnp.concatenate(
            [jnp.where(even, from_odd, from_even), cells, jnp.where(even, from_even, from_odd)],
            axis=dim,
        )
    return cells


def swapped(head, tail, axis):
    count = lax.axis_size(axis)
    even = lax.axis_index(axis) % 2 == 0
    edges = {
        parity: [(i, i + 1) for i in range(parity, count - 1, 2)]
        + [(i + 1, i) for i in range(parity, count - 1, 2)]
        for parity in (0, 1)
    }
    from_even = lax.ppermute(jnp.where(even, tail, head), axis, edges[0])
    from_odd = lax.ppermute(jnp.where(even, head, tail), axis, edges[1])
    return jnp.where(even, from_odd, from_even), jnp.where(even, from_even, from_odd)


def make_kernel(spread_diff, offsets, w_emit, w_absorb):
    kernel = jnp.sum(
        jnp.where(spread_diff[:, :, None] == offsets, w_emit, jnp.float32(0.0)), axis=2
    )
    return kernel + jnp.sum(
        jnp.where(spread_diff[:, :, None] == -offsets, w_absorb, jnp.float32(0.0)), axis=2
    )


def coupled_blocks(window, coupling, local_ids):
    f32, bf16 = jnp.float32, jnp.bfloat16
    nwin = window.shape[0]
    onehot = (local_ids[:, :, None] == jnp.arange(nwin, dtype=local_ids.dtype)).astype(bf16)
    mr = coupling[:, :, 0]
    mi = coupling[:, :, 1]
    mbig = jnp.stack([jnp.stack([mr, -mi], axis=2), jnp.stack([mi, mr], axis=2)], axis=2)
    left = mbig[:, :, :, None] * onehot[:, :, None, :, None, None, None]
    x = jnp.einsum("akqwpij,wpjle->akqile", left, window, preferred_element_type=f32).astype(bf16)
    x = x.transpose(0, 1, 2, 4, 3, 5)
    right = jnp.stack([jnp.stack([mr, mi], axis=2), jnp.stack([-mi, mr], axis=2)], axis=2)
    return jnp.einsum("akplie,akqpml->aqime", x, right, preferred_element_type=f32)


def shards(green, coupling, neighbours, offsets, w_emit, w_absorb):
    hi = lax.Precision.HIGHEST
    atoms_here = green.shape[0]
    points = green.shape[-1]
    reach = points * 3 // 8
    window = extended(green, (("atom", 0),), atoms_here)
    local_ids = neighbours - (lax.axis_index("atom") - 1) * atoms_here
    extent = points + 2 * reach
    spread_diff = (
        jnp.arange(extent, dtype=jnp.int32)[:, None]
        - reach
        - jnp.arange(points, dtype=jnp.int32)[None, :]
    )
    kernel = make_kernel(spread_diff, offsets, w_emit, w_absorb)
    coupled = coupled_blocks(window, coupling, local_ids)
    coupled, kernel = lax.optimization_barrier((coupled, kernel))
    rows = coupled.size // points
    flat = coupled.reshape(rows, points)
    packed = (rows * reach) // 128

    def pack(part):
        return part.astype(jnp.bfloat16).reshape(packed, 128)

    def unpack(part):
        return part.reshape(rows, reach).astype(jnp.float32)

    lower, upper = swapped(pack(flat[:, :reach]), pack(flat[:, points - reach:]), "energy")
    widened = jnp.concatenate([unpack(lower), flat, unpack(upper)], axis=1)
    result = jnp.dot(
        widened.reshape(-1, extent), kernel, precision=hi, preferred_element_type=jnp.float32
    )
    return result.reshape(coupled.shape)


def solution(mesh):
    return jax.shard_map(
        shards,
        mesh=mesh,
        in_specs=(
            P("atom", None, None, None, "energy"),
            P("atom", None, None, None, None),
            P("atom", None),
            P(),
            P(),
            P(),
        ),
        out_specs=P("atom", None, None, None, "energy"),
        check_vma=False,
    )
```

```python
import jax
import jax.numpy as jnp
from jax import lax
from jax.sharding import PartitionSpec as P


def extended(cells, sides, width):
    for axis, dim in sides:
        count = lax.axis_size(axis)
        even = lax.axis_index(axis) % 2 == 0
        head = lax.slice_in_dim(cells, 0, width, axis=dim)
        tail = lax.slice_in_dim(cells, cells.shape[dim] - width, cells.shape[dim], axis=dim)
        edges = {
            parity: [(i, i + 1) for i in range(parity, count - 1, 2)]
            + [(i + 1, i) for i in range(parity, count - 1, 2)]
            for parity in (0, 1)
        }
        from_even = lax.ppermute(jnp.where(even, tail, head), axis, edges[0])
        from_odd = lax.ppermute(jnp.where(even, head, tail), axis, edges[1])
        cells = jnp.concatenate(
            [jnp.where(even, from_odd, from_even), cells, jnp.where(even, from_even, from_odd)],
            axis=dim,
        )
    return cells


def swapped(head, tail, axis):
    count = lax.axis_size(axis)
    even = lax.axis_index(axis) % 2 == 0
    edges = {
        parity: [(i, i + 1) for i in range(parity, count - 1, 2)]
        + [(i + 1, i) for i in range(parity, count - 1, 2)]
        for parity in (0, 1)
    }
    from_even = lax.ppermute(jnp.where(even, tail, head), axis, edges[0])
    from_odd = lax.ppermute(jnp.where(even, head, tail), axis, edges[1])
    return jnp.where(even, from_odd, from_even), jnp.where(even, from_even, from_odd)


def make_kernel(spread_diff, offsets, w_emit, w_absorb):
    kernel = jnp.sum(
        jnp.where(spread_diff[:, :, None] == offsets, w_emit, jnp.float32(0.0)), axis=2
    )
    return kernel + jnp.sum(
        jnp.where(spread_diff[:, :, None] == -offsets, w_absorb, jnp.float32(0.0)), axis=2
    )


def coupled_blocks(window, coupling, local_ids):
    f32, bf16 = jnp.float32, jnp.bfloat16
    nwin = window.shape[1]
    atoms, nb, _, orb, _ = coupling.shape
    onehot = (local_ids[:, :, None] == jnp.arange(nwin, dtype=local_ids.dtype)).astype(bf16)
    mr = coupling[:, :, 0]
    mi = coupling[:, :, 1]
    mbig = jnp.stack([jnp.stack([mr, -mi], axis=4), jnp.stack([mi, mr], axis=4)], axis=2)
    mbig = mbig.reshape(atoms, nb, 2, orb, 2 * orb)
    left = mbig[:, :, :, None] * onehot[:, :, None, :, None, None]
    x = jnp.einsum("akqwis,lwse->akqile", left, window, preferred_element_type=f32).astype(bf16)
    x = x.transpose(0, 1, 2, 4, 3, 5)
    right = jnp.stack([jnp.stack([mr, mi], axis=2), jnp.stack([-mi, mr], axis=2)], axis=2)
    return jnp.einsum("akplie,akqpml->aqime", x, right, preferred_element_type=f32)


def shards(green, coupling, neighbours, offsets, w_emit, w_absorb):
    hi = lax.Precision.HIGHEST
    atoms_here = green.shape[0]
    points = green.shape[-1]
    reach = points * 3 // 8
    merged = green.transpose(3, 0, 2, 1, 4).reshape(green.shape[3], atoms_here, -1, points)
    window = extended(merged, (("atom", 1),), atoms_here)
    local_ids = neighbours - (lax.axis_index("atom") - 1) * atoms_here
    extent = points + 2 * reach
    spread_diff = (
        jnp.arange(extent, dtype=jnp.int32)[:, None]
        - reach
        - jnp.arange(points, dtype=jnp.int32)[None, :]
    )
    kernel = make_kernel(spread_diff, offsets, w_emit, w_absorb)
    coupled = coupled_blocks(window, coupling, local_ids)
    coupled, kernel = lax.optimization_barrier((coupled, kernel))
    rows = coupled.size // points
    flat = coupled.reshape(rows, points)
    packed = (rows * reach) // 128

    def pack(part):
        return part.astype(jnp.bfloat16).reshape(packed, 128)

    def unpack(part):
        return part.reshape(rows, reach).astype(jnp.float32)

    lower, upper = swapped(pack(flat[:, :reach]), pack(flat[:, points - reach:]), "energy")
    widened = jnp.concatenate([unpack(lower), flat, unpack(upper)], axis=1)
    result = jnp.dot(
        widened.reshape(-1, extent), kernel, precision=hi, preferred_element_type=jnp.float32
    )
    return result.reshape(coupled.shape)


def solution(mesh):
    return jax.shard_map(
        shards,
        mesh=mesh,
        in_specs=(
            P("atom", None, None, None, "energy"),
            P("atom", None, None, None, None),
            P("atom", None),
            P(),
            P(),
            P(),
        ),
        out_specs=P("atom", None, None, None, "energy"),
        check_vma=False,
    )
```

```python
import jax
import jax.numpy as jnp
from jax import lax
from jax.sharding import PartitionSpec as P


def extended(cells, sides, width):
    for axis, dim in sides:
        count = lax.axis_size(axis)
        even = lax.axis_index(axis) % 2 == 0
        head = lax.slice_in_dim(cells, 0, width, axis=dim)
        tail = lax.slice_in_dim(cells, cells.shape[dim] - width, cells.shape[dim], axis=dim)
        edges = {
            parity: [(i, i + 1) for i in range(parity, count - 1, 2)]
            + [(i + 1, i) for i in range(parity, count - 1, 2)]
            for parity in (0, 1)
        }
        from_even = lax.ppermute(jnp.where(even, tail, head), axis, edges[0])
        from_odd = lax.ppermute(jnp.where(even, head, tail), axis, edges[1])
        cells = jnp.concatenate(
            [jnp.where(even, from_odd, from_even), cells, jnp.where(even, from_even, from_odd)],
            axis=dim,
        )
    return cells


def swapped(head, tail, axis, between=None):
    count = lax.axis_size(axis)
    even = lax.axis_index(axis) % 2 == 0
    edges = {
        parity: [(i, i + 1) for i in range(parity, count - 1, 2)]
        + [(i + 1, i) for i in range(parity, count - 1, 2)]
        for parity in (0, 1)
    }
    from_even = lax.ppermute(jnp.where(even, tail, head), axis, edges[0])
    second = jnp.where(even, head, tail)
    if between is not None:
        second, _ = lax.optimization_barrier((second, between))
    from_odd = lax.ppermute(second, axis, edges[1])
    return jnp.where(even, from_odd, from_even), jnp.where(even, from_even, from_odd)


def make_kernel(spread_diff, offsets, w_emit, w_absorb):
    kernel = jnp.sum(
        jnp.where(spread_diff[:, :, None] == offsets, w_emit, jnp.float32(0.0)), axis=2
    )
    return kernel + jnp.sum(
        jnp.where(spread_diff[:, :, None] == -offsets, w_absorb, jnp.float32(0.0)), axis=2
    )


def coupled_blocks(window, coupling, local_ids):
    f32, bf16 = jnp.float32, jnp.bfloat16
    nwin = window.shape[1]
    atoms, nb, _, orb, _ = coupling.shape
    onehot = (local_ids[:, :, None] == jnp.arange(nwin, dtype=local_ids.dtype)).astype(bf16)
    mr = coupling[:, :, 0]
    mi = coupling[:, :, 1]
    mbig = jnp.stack([jnp.stack([mr, -mi], axis=4), jnp.stack([mi, mr], axis=4)], axis=2)
    mbig = mbig.reshape(atoms, nb, 2, orb, 2 * orb)
    left = mbig[:, :, :, None] * onehot[:, :, None, :, None, None]
    x = jnp.einsum("akqwis,lwse->akqile", left, window, preferred_element_type=f32).astype(bf16)
    x = x.transpose(0, 1, 2, 4, 3, 5)
    right = jnp.stack([jnp.stack([mr, mi], axis=2), jnp.stack([-mi, mr], axis=2)], axis=2)
    return jnp.einsum("akplie,akqpml->aqime", x, right, preferred_element_type=f32)


def shards(green, coupling, neighbours, offsets, w_emit, w_absorb):
    hi = lax.Precision.HIGHEST
    atoms_here = green.shape[0]
    points = green.shape[-1]
    reach = points * 3 // 8
    merged = green.transpose(3, 0, 2, 1, 4).reshape(green.shape[3], atoms_here, -1, points)
    extent = points + 2 * reach
    spread_diff = (
        jnp.arange(extent, dtype=jnp.int32)[:, None]
        - reach
        - jnp.arange(points, dtype=jnp.int32)[None, :]
    )
    kernel = make_kernel(spread_diff, offsets, w_emit, w_absorb)
    before, after = swapped(merged, merged, "atom", kernel)
    window = jnp.concatenate([before, merged, after], axis=1)
    local_ids = neighbours - (lax.axis_index("atom") - 1) * atoms_here
    coupled = coupled_blocks(window, coupling, local_ids)
    coupled, kernel = lax.optimization_barrier((coupled, kernel))
    rows = coupled.size // points
    flat = coupled.reshape(rows, points)
    packed = (rows * reach) // 128

    def pack(part):
        return part.astype(jnp.bfloat16).reshape(packed, 128)

    def unpack(part):
        return part.reshape(rows, reach).astype(jnp.float32)

    lower, upper = swapped(pack(flat[:, :reach]), pack(flat[:, points - reach:]), "energy")
    widened = jnp.concatenate([unpack(lower), flat, unpack(upper)], axis=1)
    result = jnp.dot(
        widened.reshape(-1, extent), kernel, precision=hi, preferred_element_type=jnp.float32
    )
    return result.reshape(coupled.shape)


def solution(mesh):
    return jax.shard_map(
        shards,
        mesh=mesh,
        in_specs=(
            P("atom", None, None, None, "energy"),
            P("atom", None, None, None, None),
            P("atom", None),
            P(),
            P(),
            P(),
        ),
        out_specs=P("atom", None, None, None, "energy"),
        check_vma=False,
    )
```

```python
import jax
import jax.numpy as jnp
from jax import lax
from jax.sharding import PartitionSpec as P


def swapped(head, tail, axis):
    count = lax.axis_size(axis)
    index = lax.axis_index(axis)
    even = index % 2 == 0
    pairs = {parity: [(i, (i + 1) % count) for i in range(parity, count - 1 + parity, 2)] for parity in (0, 1)}
    edges = {parity: pairs[parity] + [(b, a) for a, b in pairs[parity]] for parity in (0, 1)}
    from_even = lax.ppermute(jnp.where(even, tail, head), axis, edges[0])
    from_odd = lax.ppermute(jnp.where(even, head, tail), axis, edges[1])
    lower = jnp.where(even, from_odd, from_even)
    upper = jnp.where(even, from_even, from_odd)
    lower = jnp.where(index == 0, jnp.zeros_like(lower), lower)
    upper = jnp.where(index == count - 1, jnp.zeros_like(upper), upper)
    return lower, upper


def make_kernel(spread_diff, offsets, w_emit, w_absorb):
    kernel = jnp.sum(
        jnp.where(spread_diff[:, :, None] == offsets, w_emit, jnp.float32(0.0)), axis=2
    )
    return kernel + jnp.sum(
        jnp.where(spread_diff[:, :, None] == -offsets, w_absorb, jnp.float32(0.0)), axis=2
    )


def coupled_blocks(window, coupling, local_ids):
    f32, bf16 = jnp.float32, jnp.bfloat16
    nwin = window.shape[1]
    atoms, nb, _, orb, _ = coupling.shape
    onehot = (local_ids[:, :, None] == jnp.arange(nwin, dtype=local_ids.dtype)).astype(bf16)
    mr = coupling[:, :, 0]
    mi = coupling[:, :, 1]
    mbig = jnp.stack([jnp.stack([mr, -mi], axis=4), jnp.stack([mi, mr], axis=4)], axis=2)
    mbig = mbig.reshape(atoms, nb, 2, orb, 2 * orb)
    left = mbig[:, :, :, None] * onehot[:, :, None, :, None, None]
    x = jnp.einsum("akqwis,lwse->akqile", left, window, preferred_element_type=f32).astype(bf16)
    x = x.transpose(0, 1, 2, 4, 3, 5)
    right = jnp.stack([jnp.stack([mr, mi], axis=2), jnp.stack([-mi, mr], axis=2)], axis=2)
    return jnp.einsum("akplie,akqpml->aqime", x, right, preferred_element_type=f32)


def shards(green, coupling, neighbours, offsets, w_emit, w_absorb):
    hi = lax.Precision.HIGHEST
    atoms_here = green.shape[0]
    points = green.shape[-1]
    reach = points * 3 // 8
    merged = green.transpose(3, 0, 2, 1, 4).reshape(green.shape[3], atoms_here, -1, points)
    before, after = swapped(merged, merged, "atom")
    window = jnp.concatenate([before, merged, after], axis=1)
    local_ids = neighbours - (lax.axis_index("atom") - 1) * atoms_here
    extent = points + 2 * reach
    spread_diff = (
        jnp.arange(extent, dtype=jnp.int32)[:, None]
        - reach
        - jnp.arange(points, dtype=jnp.int32)[None, :]
    )
    kernel = make_kernel(spread_diff, offsets, w_emit, w_absorb)
    coupled = coupled_blocks(window, coupling, local_ids)
    coupled, kernel = lax.optimization_barrier((coupled, kernel))
    rows = coupled.size // points
    flat = coupled.reshape(rows, points)
    packed = (rows * reach) // 128

    def pack(part):
        return part.astype(jnp.bfloat16).reshape(packed, 128)

    def unpack(part):
        return part.reshape(rows, reach).astype(jnp.float32)

    lower, upper = swapped(pack(flat[:, :reach]), pack(flat[:, points - reach:]), "energy")
    widened = jnp.concatenate([unpack(lower), flat, unpack(upper)], axis=1)
    result = jnp.dot(
        widened.reshape(-1, extent), kernel, precision=hi, preferred_element_type=jnp.float32
    )
    return result.reshape(coupled.shape)


def solution(mesh):
    return jax.shard_map(
        shards,
        mesh=mesh,
        in_specs=(
            P("atom", None, None, None, "energy"),
            P("atom", None, None, None, None),
            P("atom", None),
            P(),
            P(),
            P(),
        ),
        out_specs=P("atom", None, None, None, "energy"),
        check_vma=False,
    )
```

```python
import jax
import jax.numpy as jnp
from jax import lax
from jax.sharding import PartitionSpec as P


def extended(cells, sides, width):
    for axis, dim in sides:
        count = lax.axis_size(axis)
        even = lax.axis_index(axis) % 2 == 0
        head = lax.slice_in_dim(cells, 0, width, axis=dim)
        tail = lax.slice_in_dim(cells, cells.shape[dim] - width, cells.shape[dim], axis=dim)
        edges = {
            parity: [(i, i + 1) for i in range(parity, count - 1, 2)]
            + [(i + 1, i) for i in range(parity, count - 1, 2)]
            for parity in (0, 1)
        }
        from_even = lax.ppermute(jnp.where(even, tail, head), axis, edges[0])
        from_odd = lax.ppermute(jnp.where(even, head, tail), axis, edges[1])
        cells = jnp.concatenate(
            [jnp.where(even, from_odd, from_even), cells, jnp.where(even, from_even, from_odd)],
            axis=dim,
        )
    return cells


def swapped(head, tail, axis):
    count = lax.axis_size(axis)
    even = lax.axis_index(axis) % 2 == 0
    edges = {
        parity: [(i, i + 1) for i in range(parity, count - 1, 2)]
        + [(i + 1, i) for i in range(parity, count - 1, 2)]
        for parity in (0, 1)
    }
    from_even = lax.ppermute(jnp.where(even, tail, head), axis, edges[0])
    from_odd = lax.ppermute(jnp.where(even, head, tail), axis, edges[1])
    return jnp.where(even, from_odd, from_even), jnp.where(even, from_even, from_odd)


def make_kernel(spread_diff, offsets, w_emit, w_absorb):
    kernel = jnp.sum(
        jnp.where(spread_diff[:, :, None] == offsets, w_emit, jnp.float32(0.0)), axis=2
    )
    return kernel + jnp.sum(
        jnp.where(spread_diff[:, :, None] == -offsets, w_absorb, jnp.float32(0.0)), axis=2
    )


def coupled_blocks(window, coupling, local_ids):
    f32, bf16 = jnp.float32, jnp.bfloat16
    nwin = window.shape[1]
    atoms, nb, _, orb, _ = coupling.shape
    onehot = (local_ids[:, :, None] == jnp.arange(nwin, dtype=local_ids.dtype)).astype(bf16)
    mr = coupling[:, :, 0]
    mi = coupling[:, :, 1]
    mbig = jnp.stack([jnp.stack([mr, -mi], axis=4), jnp.stack([mi, mr], axis=4)], axis=2)
    mbig = mbig.reshape(atoms, nb, 2, orb, 2 * orb)
    left = mbig[:, :, :, None] * onehot[:, :, None, :, None, None]
    x = jnp.einsum("akqwis,lwse->akqile", left, window, preferred_element_type=f32).astype(bf16)
    x = x.transpose(0, 1, 2, 4, 3, 5)
    right = jnp.stack([jnp.stack([mr, mi], axis=2), jnp.stack([-mi, mr], axis=2)], axis=2)
    return jnp.einsum("akplie,akqpml->aqime", x, right, preferred_element_type=f32)


def shards(green, coupling, neighbours, offsets, w_emit, w_absorb):
    hi = lax.Precision.HIGHEST
    atoms_here = green.shape[0]
    points = green.shape[-1]
    reach = points * 3 // 8
    merged = green.transpose(3, 0, 2, 1, 4).reshape(green.shape[3], atoms_here, -1, points)
    window = extended(merged, (("atom", 1),), atoms_here)
    local_ids = neighbours - (lax.axis_index("atom") - 1) * atoms_here
    extent = points + 2 * reach
    spread_diff = (
        jnp.arange(extent, dtype=jnp.int32)[:, None]
        - reach
        - jnp.arange(points, dtype=jnp.int32)[None, :]
    )
    kernel = make_kernel(spread_diff, offsets, w_emit, w_absorb)
    coupled = coupled_blocks(window, coupling, local_ids)
    coupled, kernel = lax.optimization_barrier((coupled, kernel))
    rows = coupled.size // points
    flat = coupled.reshape(rows, points)
    packed = (rows * reach) // 128

    def pack(part):
        return part.astype(jnp.bfloat16).reshape(packed, 128)

    def unpack(part):
        return part.reshape(rows, reach).astype(jnp.float32)

    lower, upper = swapped(pack(flat[:, :reach]), pack(flat[:, points - reach:]), "energy")
    result = jnp.dot(flat, kernel[reach:reach + points], precision=hi, preferred_element_type=jnp.float32)
    result = result + jnp.dot(
        unpack(lower), kernel[:reach], precision=hi, preferred_element_type=jnp.float32
    )
    result = result + jnp.dot(
        unpack(upper), kernel[reach + points:], precision=hi, preferred_element_type=jnp.float32
    )
    return result.reshape(coupled.shape)


def solution(mesh):
    return jax.shard_map(
        shards,
        mesh=mesh,
        in_specs=(
            P("atom", None, None, None, "energy"),
            P("atom", None, None, None, None),
            P("atom", None),
            P(),
            P(),
            P(),
        ),
        out_specs=P("atom", None, None, None, "energy"),
        check_vma=False,
    )
```

```python
import jax
import jax.numpy as jnp
from jax import lax
from jax.sharding import PartitionSpec as P


def extended(cells, sides, width):
    for axis, dim in sides:
        count = lax.axis_size(axis)
        even = lax.axis_index(axis) % 2 == 0
        head = lax.slice_in_dim(cells, 0, width, axis=dim)
        tail = lax.slice_in_dim(cells, cells.shape[dim] - width, cells.shape[dim], axis=dim)
        edges = {
            parity: [(i, i + 1) for i in range(parity, count - 1, 2)]
            + [(i + 1, i) for i in range(parity, count - 1, 2)]
            for parity in (0, 1)
        }
        from_even = lax.ppermute(jnp.where(even, tail, head), axis, edges[0])
        from_odd = lax.ppermute(jnp.where(even, head, tail), axis, edges[1])
        cells = jnp.concatenate(
            [jnp.where(even, from_odd, from_even), cells, jnp.where(even, from_even, from_odd)],
            axis=dim,
        )
    return cells


def swapped(head, tail, axis):
    count = lax.axis_size(axis)
    even = lax.axis_index(axis) % 2 == 0
    edges = {
        parity: [(i, i + 1) for i in range(parity, count - 1, 2)]
        + [(i + 1, i) for i in range(parity, count - 1, 2)]
        for parity in (0, 1)
    }
    from_even = lax.ppermute(jnp.where(even, tail, head), axis, edges[0])
    from_odd = lax.ppermute(jnp.where(even, head, tail), axis, edges[1])
    return jnp.where(even, from_odd, from_even), jnp.where(even, from_even, from_odd)


def make_kernel(spread_diff, offsets, w_emit, w_absorb):
    kernel = jnp.sum(
        jnp.where(spread_diff[:, :, None] == offsets, w_emit, jnp.float32(0.0)), axis=2
    )
    return kernel + jnp.sum(
        jnp.where(spread_diff[:, :, None] == -offsets, w_absorb, jnp.float32(0.0)), axis=2
    )


def coupled_blocks(window, coupling, local_ids):
    f32, bf16 = jnp.float32, jnp.bfloat16
    nwin = window.shape[1]
    atoms, nb, _, orb, _ = coupling.shape
    onehot = (local_ids[:, :, None] == jnp.arange(nwin, dtype=local_ids.dtype)).astype(bf16)
    mr = coupling[:, :, 0]
    mi = coupling[:, :, 1]
    mbig = jnp.stack([jnp.stack([mr, -mi], axis=4), jnp.stack([mi, mr], axis=4)], axis=2)
    mbig = mbig.reshape(atoms, nb, 2, orb, 2 * orb)
    left = mbig[:, :, :, None] * onehot[:, :, None, :, None, None]
    x = jnp.einsum("akqwis,lwse->akqile", left, window, preferred_element_type=f32).astype(bf16)
    x = x.transpose(0, 1, 2, 4, 3, 5)
    right = jnp.stack([jnp.stack([mr, mi], axis=2), jnp.stack([-mi, mr], axis=2)], axis=2)
    return jnp.einsum("akplie,akqpml->aqime", x, right, preferred_element_type=f32)


def shards(green, coupling, neighbours, offsets, w_emit, w_absorb):
    hi = lax.Precision.HIGH
    atoms_here = green.shape[0]
    points = green.shape[-1]
    reach = points * 3 // 8
    merged = green.transpose(3, 0, 2, 1, 4).reshape(green.shape[3], atoms_here, -1, points)
    window = extended(merged, (("atom", 1),), atoms_here)
    local_ids = neighbours - (lax.axis_index("atom") - 1) * atoms_here
    extent = points + 2 * reach
    spread_diff = (
        jnp.arange(extent, dtype=jnp.int32)[:, None]
        - reach
        - jnp.arange(points, dtype=jnp.int32)[None, :]
    )
    kernel = make_kernel(spread_diff, offsets, w_emit, w_absorb)
    coupled = coupled_blocks(window, coupling, local_ids)
    coupled, kernel = lax.optimization_barrier((coupled, kernel))
    rows = coupled.size // points
    flat = coupled.reshape(rows, points)
    packed = (rows * reach) // 128

    def pack(part):
        return part.astype(jnp.bfloat16).reshape(packed, 128)

    def unpack(part):
        return part.reshape(rows, reach).astype(jnp.float32)

    lower, upper = swapped(pack(flat[:, :reach]), pack(flat[:, points - reach:]), "energy")
    result = jnp.dot(flat, kernel[reach:reach + points], precision=hi, preferred_element_type=jnp.float32)
    result = result + jnp.dot(
        unpack(lower), kernel[:reach], precision=hi, preferred_element_type=jnp.float32
    )
    result = result + jnp.dot(
        unpack(upper), kernel[reach + points:], precision=hi, preferred_element_type=jnp.float32
    )
    return result.reshape(coupled.shape)


def solution(mesh):
    return jax.shard_map(
        shards,
        mesh=mesh,
        in_specs=(
            P("atom", None, None, None, "energy"),
            P("atom", None, None, None, None),
            P("atom", None),
            P(),
            P(),
            P(),
        ),
        out_specs=P("atom", None, None, None, "energy"),
        check_vma=False,
    )
```

```python
import jax
import jax.numpy as jnp
from jax import lax
from jax.sharding import PartitionSpec as P


def extended(cells, sides, width):
    for axis, dim in sides:
        count = lax.axis_size(axis)
        even = lax.axis_index(axis) % 2 == 0
        head = lax.slice_in_dim(cells, 0, width, axis=dim)
        tail = lax.slice_in_dim(cells, cells.shape[dim] - width, cells.shape[dim], axis=dim)
        edges = {
            parity: [(i, i + 1) for i in range(parity, count - 1, 2)]
            + [(i + 1, i) for i in range(parity, count - 1, 2)]
            for parity in (0, 1)
        }
        from_even = lax.ppermute(jnp.where(even, tail, head), axis, edges[0])
        from_odd = lax.ppermute(jnp.where(even, head, tail), axis, edges[1])
        cells = jnp.concatenate(
            [jnp.where(even, from_odd, from_even), cells, jnp.where(even, from_even, from_odd)],
            axis=dim,
        )
    return cells


def swapped(head, tail, axis):
    count = lax.axis_size(axis)
    even = lax.axis_index(axis) % 2 == 0
    edges = {
        parity: [(i, i + 1) for i in range(parity, count - 1, 2)]
        + [(i + 1, i) for i in range(parity, count - 1, 2)]
        for parity in (0, 1)
    }
    from_even = lax.ppermute(jnp.where(even, tail, head), axis, edges[0])
    from_odd = lax.ppermute(jnp.where(even, head, tail), axis, edges[1])
    return jnp.where(even, from_odd, from_even), jnp.where(even, from_even, from_odd)


def make_kernel(spread_diff, offsets, w_emit, w_absorb):
    kernel = jnp.sum(
        jnp.where(spread_diff[:, :, None] == offsets, w_emit, jnp.float32(0.0)), axis=2
    )
    return kernel + jnp.sum(
        jnp.where(spread_diff[:, :, None] == -offsets, w_absorb, jnp.float32(0.0)), axis=2
    )


def coupled_blocks(window, coupling, local_ids):
    f32, bf16 = jnp.float32, jnp.bfloat16
    nwin = window.shape[1]
    atoms, nb, _, orb, _ = coupling.shape
    onehot = (local_ids[:, :, None] == jnp.arange(nwin, dtype=local_ids.dtype)).astype(bf16)
    mr = coupling[:, :, 0]
    mi = coupling[:, :, 1]
    mbig = jnp.stack([jnp.stack([mr, -mi], axis=4), jnp.stack([mi, mr], axis=4)], axis=2)
    mbig = mbig.reshape(atoms, nb, 2, orb, 2 * orb)
    left = mbig[:, :, :, None] * onehot[:, :, None, :, None, None]
    x = jnp.einsum("akqwis,lwse->akqile", left, window, preferred_element_type=f32).astype(bf16)
    x = x.transpose(0, 1, 2, 4, 3, 5)
    right = jnp.stack([jnp.stack([mr, mi], axis=2), jnp.stack([-mi, mr], axis=2)], axis=2)
    return jnp.einsum("akplie,akqpml->aimqe", x, right, preferred_element_type=f32)


def shards(green, coupling, neighbours, offsets, w_emit, w_absorb):
    hi = lax.Precision.HIGH
    atoms_here = green.shape[0]
    points = green.shape[-1]
    reach = points * 3 // 8
    merged = green.transpose(3, 0, 2, 1, 4).reshape(green.shape[3], atoms_here, -1, points)
    window = extended(merged, (("atom", 1),), atoms_here)
    local_ids = neighbours - (lax.axis_index("atom") - 1) * atoms_here
    extent = points + 2 * reach
    spread_diff = (
        jnp.arange(extent, dtype=jnp.int32)[:, None]
        - reach
        - jnp.arange(points, dtype=jnp.int32)[None, :]
    )
    kernel = make_kernel(spread_diff, offsets, w_emit, w_absorb)
    coupled = coupled_blocks(window, coupling, local_ids)
    coupled, kernel = lax.optimization_barrier((coupled, kernel))
    rows = coupled.size // points
    flat = coupled.reshape(rows, points)
    packed = (rows * reach) // 128

    def pack(part):
        return part.astype(jnp.bfloat16).reshape(packed, 128)

    def unpack(part):
        return part.reshape(rows, reach).astype(jnp.float32)

    lower, upper = swapped(pack(flat[:, :reach]), pack(flat[:, points - reach:]), "energy")
    result = jnp.dot(flat, kernel[reach:reach + points], precision=hi, preferred_element_type=jnp.float32)
    result = result + jnp.dot(
        unpack(lower), kernel[:reach], precision=hi, preferred_element_type=jnp.float32
    )
    result = result + jnp.dot(
        unpack(upper), kernel[reach + points:], precision=hi, preferred_element_type=jnp.float32
    )
    return result.reshape(coupled.shape).transpose(0, 3, 1, 2, 4)


def solution(mesh):
    return jax.shard_map(
        shards,
        mesh=mesh,
        in_specs=(
            P("atom", None, None, None, "energy"),
            P("atom", None, None, None, None),
            P("atom", None),
            P(),
            P(),
            P(),
        ),
        out_specs=P("atom", None, None, None, "energy"),
        check_vma=False,
    )
```

```python
import jax
import jax.numpy as jnp
from jax import lax
from jax.sharding import PartitionSpec as P


def extended(cells, sides, width):
    for axis, dim in sides:
        count = lax.axis_size(axis)
        even = lax.axis_index(axis) % 2 == 0
        head = lax.slice_in_dim(cells, 0, width, axis=dim)
        tail = lax.slice_in_dim(cells, cells.shape[dim] - width, cells.shape[dim], axis=dim)
        edges = {
            parity: [(i, i + 1) for i in range(parity, count - 1, 2)]
            + [(i + 1, i) for i in range(parity, count - 1, 2)]
            for parity in (0, 1)
        }
        from_even = lax.ppermute(jnp.where(even, tail, head), axis, edges[0])
        from_odd = lax.ppermute(jnp.where(even, head, tail), axis, edges[1])
        cells = jnp.concatenate(
            [jnp.where(even, from_odd, from_even), cells, jnp.where(even, from_even, from_odd)],
            axis=dim,
        )
    return cells


def swapped(head, tail, axis):
    count = lax.axis_size(axis)
    even = lax.axis_index(axis) % 2 == 0
    edges = {
        parity: [(i, i + 1) for i in range(parity, count - 1, 2)]
        + [(i + 1, i) for i in range(parity, count - 1, 2)]
        for parity in (0, 1)
    }
    from_even = lax.ppermute(jnp.where(even, tail, head), axis, edges[0])
    from_odd = lax.ppermute(jnp.where(even, head, tail), axis, edges[1])
    return jnp.where(even, from_odd, from_even), jnp.where(even, from_even, from_odd)


def make_kernel(spread_diff, offsets, w_emit, w_absorb):
    kernel = jnp.sum(
        jnp.where(spread_diff[:, :, None] == offsets, w_emit, jnp.float32(0.0)), axis=2
    )
    return kernel + jnp.sum(
        jnp.where(spread_diff[:, :, None] == -offsets, w_absorb, jnp.float32(0.0)), axis=2
    )


def coupled_blocks(window, coupling, local_ids):
    f32, bf16 = jnp.float32, jnp.bfloat16
    nwin = window.shape[1]
    atoms, nb, _, orb, _ = coupling.shape
    onehot = (local_ids[:, :, None] == jnp.arange(nwin, dtype=local_ids.dtype)).astype(bf16)
    mr = coupling[:, :, 0]
    mi = coupling[:, :, 1]
    mbig = jnp.stack([jnp.stack([mr, -mi], axis=4), jnp.stack([mi, mr], axis=4)], axis=2)
    mbig = mbig.reshape(atoms, nb, 2, orb, 2 * orb)
    left = mbig[:, :, :, None] * onehot[:, :, None, :, None, None]
    x = jnp.einsum("akqwis,lwse->akqile", left, window, preferred_element_type=f32).astype(bf16)
    x = x.transpose(0, 1, 2, 4, 3, 5)
    right = jnp.stack([jnp.stack([mr, mi], axis=2), jnp.stack([-mi, mr], axis=2)], axis=2)
    return jnp.einsum("akplie,akqpml->aimqe", x, right, preferred_element_type=f32)


def shards(green, coupling, neighbours, offsets, w_emit, w_absorb):
    hi = lax.Precision.HIGH
    atoms_here = green.shape[0]
    points = green.shape[-1]
    reach = points * 3 // 8
    merged = green.transpose(3, 0, 2, 1, 4).reshape(green.shape[3], atoms_here, -1, points)
    window = extended(merged, (("atom", 1),), atoms_here)
    local_ids = neighbours - (lax.axis_index("atom") - 1) * atoms_here
    extent = points + 2 * reach
    spread_diff = (
        jnp.arange(extent, dtype=jnp.int32)[:, None]
        - reach
        - jnp.arange(points, dtype=jnp.int32)[None, :]
    )
    kernel = make_kernel(spread_diff, offsets, w_emit, w_absorb)
    coupled = coupled_blocks(window, coupling, local_ids)
    coupled, kernel = lax.optimization_barrier((coupled, kernel))
    rows = coupled.size // points
    flat = coupled.reshape(rows, points)
    packed = (rows * reach) // 128

    def pack(part):
        return part.astype(jnp.bfloat16).reshape(packed, 128)

    def unpack(part):
        return part.reshape(rows, reach).astype(jnp.float32)

    lower, upper = swapped(pack(flat[:, :reach]), pack(flat[:, points - reach:]), "energy")
    result = jnp.dot(flat, kernel[reach:reach + points], precision=hi, preferred_element_type=jnp.float32)
    for halo, block in ((lower, kernel[:reach]), (upper, kernel[reach + points:])):
        block_hi = block.astype(jnp.bfloat16)
        block_lo = (block - block_hi.astype(jnp.float32)).astype(jnp.bfloat16)
        values = halo.reshape(rows, reach)
        result = result + jnp.dot(values, block_hi, preferred_element_type=jnp.float32)
        result = result + jnp.dot(values, block_lo, preferred_element_type=jnp.float32)
    return result.reshape(coupled.shape).transpose(0, 3, 1, 2, 4)


def solution(mesh):
    return jax.shard_map(
        shards,
        mesh=mesh,
        in_specs=(
            P("atom", None, None, None, "energy"),
            P("atom", None, None, None, None),
            P("atom", None),
            P(),
            P(),
            P(),
        ),
        out_specs=P("atom", None, None, None, "energy"),
        check_vma=False,
    )
```
